128 devices in a mesh: row: 16 (over z, x), col: 8 (over y, core).
Axes of the slice: x: 4, y: 4, z: 4, core: 2. Of those that a mesh axis runs over, the one named last changes fastest.
Arguments:
- psi: bfloat16 [2048, 16, 1024], P('row', None, 'col'), may hold values from -6 to 6
- env_left: bfloat16 [16, 3, 128, 128, 34], P('row'), may hold values from -0.0546875 to 0.0546875
- env_right: bfloat16 [8, 3, 128, 34, 128], P('col'), may hold values from -0.3125 to 0.3125
- first_site_operator: bfloat16 [34, 34, 4, 4], replicated, may hold values from -0.5 to 0.5
- mpo_right: bfloat16 [34, 34, 4, 4], replicated, may hold values from -0.5 to 0.5
- block_mask: int32 [16, 8], P('row', 'col'), may hold values 0 or 1
- left_live: int32 [16], P('row'), may hold values from 64 to 128, as said below
- right_live: int32 [8], P('col'), may hold values from 64 to 128, as said below
Outputs:
- hpsi: bfloat16 [2048, 16, 1024], P('row', None, 'col')
- residual: bfloat16 [2048, 16, 1024], P('row', None, 'col')
- quotient: float32 [], replicated
The draws below stay inside these ranges and needn't reach their ends.
Inputs may be any that keep to these rules, and one draw needn't show every extreme that they name: `left_live`: a block is either full or is the last block of a sector with fewer live states; some block is full. `right_live`: a block is either full or is the last block of a sector with fewer live states; some block is full.
All inputs are finite; a program needn't handle non-finite values. No bound on the sum of `block_mask` on one device may be relied on, other than what follows from the above.
Results may differ from the reference program's by a relative error of at most 0.0064.
Values may be sent and summed in bfloat16 or wider, within the bound.
No kernel may reach another device: no remote copies, remote signals or barrier semaphores. Data moves between devices by JAX's collectives and lax.ppermute only.
A program may use at most 192 MiB of HBM per device.

```python
import jax
import jax.numpy as jnp
from jax import lax

W = 34
D4 = 4
SB = 128
P_SIZE = 16
NA = 16
NB = 8
LEFT_BOND_STATES = 2048
BOND_R = 1024


def draw_sector_rows(key, amount):
    boundary = jax.random.randint(jax.random.fold_in(key, 1), (amount,), 0, 2)
    ragged = jax.random.randint(jax.random.fold_in(key, 2), (amount,), SB // 2, SB)
    chosen = jax.random.randint(jax.random.fold_in(key, 3), (), 0, amount)
    step_on = jax.random.randint(jax.random.fold_in(key, 4), (), 1, amount)
    partial_index = (chosen + step_on) % amount
    positions = jnp.arange(amount)
    values = jnp.where(boundary > 0, ragged, SB)
    values = jnp.where(positions == partial_index, SB // 2, values)
    values = jnp.where(positions == chosen, SB, values)
    return values.astype(jnp.int32)


def draw_left_live(key, part):
    return draw_sector_rows(jax.random.fold_in(key, 11), NA)


def draw_right_live(key, part):
    return draw_sector_rows(jax.random.fold_in(key, 17), NB)


def set_ends(drawn, own_key, smallest, high):
    longest = drawn.shape.index(max(drawn.shape))
    spots = []
    for shift in (0, 1):
        where = [jax.random.randint(jax.random.fold_in(own_key, axis), (), 0, length) for axis, length in enumerate(drawn.shape)]
        where[longest] = (where[longest] + shift) % drawn.shape[longest]
        spots.append(tuple(where))
    return drawn.at[spots[0]].set(smallest).at[spots[1]].set(high)


def steps_of(key, shape, split, low, high):
    factor_of, own = 1.0, jax.random.fold_in(key, 6)
    for axis_at, parts in split:
        steps = jnp.exp(jax.random.uniform(jax.random.fold_in(own, axis_at), (parts,), jnp.float32, low / len(split), high / len(split)))
        factor_of = factor_of * jnp.repeat(steps, shape[axis_at] // parts).reshape([-1 if axis == axis_at else 1 for axis in range(len(shape))])
    return factor_of


def normal_values(stream_key, extent, deviation, reach, split=(), kind=jnp.bfloat16):
    values = jax.random.normal(stream_key, extent, jnp.float32) * deviation
    if len(split) > 0:
        values = steps_of(stream_key, extent, split, -0.22, 0.18) * values
    return jnp.clip(values, min=-reach, max=reach).astype(kind)


def setup_inputs(seed: int = 0) -> dict:
    splits = jax.random.split(jax.random.key(seed), 9)
    psi = normal_values(splits[0], (LEFT_BOND_STATES, P_SIZE, BOND_R), 1.0, 6.0, ((0, 16), (2, 8)))
    env_left = normal_values(splits[1], (NA, 3, SB, SB, W), (3 * SB * W) ** -0.5, 0.0546875, ((0, 16),))
    env_right = normal_values(splits[2], (NB, 3, SB, W, SB), (3 * SB) ** -0.5, 0.3125, ((0, 8),))
    first_site_operator = normal_values(splits[3], (W, W, D4, D4), (W * D4) ** -0.5, 0.5)
    mpo_right = normal_values(splits[4], (W, W, D4, D4), (W * D4) ** -0.5, 0.5)
    block_mask = set_ends((jax.random.randint(splits[5], (NA, NB), 0, 4) < 3).astype(jnp.int32), jax.random.fold_in(splits[5], 1), 0, 1)
    left_live = draw_left_live(jax.random.fold_in(splits[8], 71), 0)
    right_live = draw_right_live(jax.random.fold_in(splits[8], 71), 0)
    return dict(psi=psi, env_left=env_left, env_right=env_right, first_site_operator=first_site_operator, mpo_right=mpo_right, block_mask=block_mask, left_live=left_live, right_live=right_live)


def reference(psi, env_left, env_right, first_site_operator, mpo_right, block_mask, left_live, right_live):
    inside = jnp.arange(SB, dtype=jnp.int32)
    row_ok = (inside[None, :] < left_live[:, None]).reshape(-1)
    col_ok = (inside[None, :] < right_live[:, None]).reshape(-1)
    expanded = jnp.repeat(jnp.repeat(block_mask, SB, axis=0), SB, axis=1)
    live_mask = (expanded > 0) & row_ok[:, None] & col_ok[None, :]
    masked_wavefunction = psi * live_mask[:, None, :].astype(psi.dtype)
    padded = jnp.pad(masked_wavefunction, ((0, 0), (0, 0), (SB, SB)))
    left_blocks = LEFT_BOND_STATES // SB

    def one_column(column):
        window = lax.dynamic_slice_in_dim(padded, column * SB, 3 * SB, 2)
        right_matrix = lax.dynamic_index_in_dim(env_right, column, 0, keepdims=False).reshape(3 * SB, W * SB)

        def one_row(position):
            strip = lax.dynamic_slice_in_dim(window, position * SB, SB, 0).reshape(SB * P_SIZE, 3 * SB)
            section_one = jnp.dot(strip, right_matrix, preferred_element_type=jnp.float32).astype(jnp.bfloat16)
            section_one = section_one.reshape(SB, D4, D4, W, SB)
            second_section = jnp.einsum("mnts,xasnb->xamtb", mpo_right.astype(jnp.float32), section_one.astype(jnp.float32)).astype(jnp.bfloat16)
            third_section = jnp.einsum("dquo,woqzj->wduzj", first_site_operator.astype(jnp.float32), second_section.astype(jnp.float32)).astype(jnp.bfloat16)
            return third_section.reshape(SB * W, P_SIZE * SB)

        outcomes = lax.map(one_row, jnp.arange(left_blocks, dtype=jnp.int32))
        zero_block = jnp.zeros((1, SB * W, P_SIZE * SB), outcomes.dtype)
        framed = jnp.concatenate([zero_block, outcomes, zero_block], axis=0)

        def one_output(position):
            couplings = lax.dynamic_index_in_dim(env_left, position, 0, keepdims=False)
            running = jnp.zeros((SB, P_SIZE * SB), jnp.float32)
            for offset in range(3):
                operand = lax.dynamic_index_in_dim(framed, position + offset, 0, keepdims=False)
                running = running + jnp.dot(couplings[offset].reshape(SB, SB * W), operand, preferred_element_type=jnp.float32)
            return running.reshape(SB, P_SIZE, SB)

        results = lax.map(one_output, jnp.arange(left_blocks, dtype=jnp.int32))
        return results.reshape(LEFT_BOND_STATES, P_SIZE, SB)

    column_list = lax.map(one_column, jnp.arange(NB, dtype=jnp.int32))
    hamiltonian_times_wavefunction = jnp.transpose(column_list, (1, 2, 0, 3)).reshape(LEFT_BOND_STATES, P_SIZE, BOND_R)
    live_float = live_mask[:, None, :].astype(jnp.float32)
    applied = hamiltonian_times_wavefunction * live_float
    psi_float = masked_wavefunction.astype(jnp.float32)
    quotient = jnp.sum(psi_float * applied) / (jnp.sum(psi_float * psi_float) + 1e-6)
    return applied.astype(jnp.bfloat16), (applied - quotient * psi_float).astype(jnp.bfloat16), quotient
```

```python
import jax
import jax.numpy as jnp
from jax import lax
from jax.sharding import PartitionSpec as P


def padded(block, sides, width):
    for axis, dim in sides:
        count = lax.axis_size(axis)
        forward = [(i, i + 1) for i in range(count - 1)]
        backward = [(target, source) for source, target in forward]
        low = lax.ppermute(
            lax.slice_in_dim(block, block.shape[dim] - width, None, axis=dim), axis, forward
        )
        high = lax.ppermute(lax.slice_in_dim(block, 0, width, axis=dim), axis, backward)
        block = jnp.concatenate([low, block, high], axis=dim)
    return block


def from_behind(block, axis, distance):
    devices = range(lax.axis_size(axis))
    route = [(i - distance, i) for i in devices if i - distance in devices]
    return lax.ppermute(block, axis, route)


def live_pattern(block_mask, left_live, right_live, block_rows):
    inside = lax.broadcasted_iota(jnp.int32, (block_rows,), 0)
    row_ok = (inside[None, :] < left_live[:, None]).reshape(-1)
    col_ok = (inside[None, :] < right_live[:, None]).reshape(-1)
    expanded = jnp.repeat(jnp.repeat(block_mask, block_rows, axis=0), block_rows, axis=1)
    return (expanded > 0) & row_ok[:, None] & col_ok[None, :]


def on_device(
    psi, env_left, env_right, first_site_operator, mpo_right, block_mask, left_live, right_live
):
    block_rows = env_left.shape[2]
    mpo_width = env_left.shape[4]
    states = psi.shape[1]
    site_states = first_site_operator.shape[2]
    couplings = env_left[0].reshape(3, block_rows, block_rows * mpo_width)
    from_next_row = from_behind(couplings[0], "row", -1)
    from_prev_row = from_behind(couplings[2], "row", 1)
    live_mask = live_pattern(block_mask, left_live, right_live, block_rows)
    masked_wavefunction = psi * live_mask[:, None, :].astype(jnp.bfloat16)
    widened = padded(masked_wavefunction, (("col", 2),), block_rows)
    right_matrix = env_right[0].reshape(3 * block_rows, mpo_width * block_rows)
    strip = widened.reshape(block_rows * states, 3 * block_rows)
    section_one = jnp.dot(strip, right_matrix, preferred_element_type=jnp.float32).astype(
        jnp.bfloat16
    )
    section_one = section_one.reshape(block_rows, site_states, site_states, mpo_width, block_rows)
    second_section = jnp.einsum(
        "mnts,xasnb->xamtb", mpo_right, section_one, preferred_element_type=jnp.float32
    ).astype(jnp.bfloat16)
    third_section = jnp.einsum(
        "dquo,woqzj->wduzj", first_site_operator, second_section, preferred_element_type=jnp.float32
    ).astype(jnp.bfloat16)
    outcome = third_section.reshape(block_rows * mpo_width, states * block_rows)

    def couple_left(coupling, operand):
        return jnp.dot(coupling, operand, preferred_element_type=jnp.float32)

    to_next = couple_left(from_next_row, outcome)
    to_prev = couple_left(from_prev_row, outcome)
    from_prev = from_behind(to_next, "row", 1)
    from_next = from_behind(to_prev, "row", -1)
    own = couple_left(couplings[1], outcome)
    total = own + from_prev + from_next
    hamiltonian_times_wavefunction = total.reshape(block_rows, states, block_rows)
    live_float = live_mask[:, None, :].astype(jnp.float32)
    applied = hamiltonian_times_wavefunction * live_float
    psi_float = masked_wavefunction.astype(jnp.float32)
    numerator, denominator = lax.psum(
        (jnp.sum(psi_float * applied), jnp.sum(psi_float * psi_float)), ("row", "col")
    )
    quotient = numerator / (denominator + 1e-06)
    return (
        applied.astype(jnp.bfloat16),
        (applied - quotient * psi_float).astype(jnp.bfloat16),
        quotient,
    )


def solution(mesh):
    return jax.shard_map(
        on_device,
        mesh=mesh,
        in_specs=(
            P("row", None, "col"),
            P("row", None, None, None, None),
            P("col", None, None, None, None),
            P(),
            P(),
            P("row", "col"),
            P("row"),
            P("col"),
        ),
        out_specs=(P("row", None, "col"), P("row", None, "col"), P()),
        check_vma=False,
    )
```

```python
import jax
import jax.numpy as jnp
from jax import lax
from jax.sharding import PartitionSpec as P


def padded(block, sides, width):
    for axis, dim in sides:
        count = lax.axis_size(axis)
        forward = [(i, i + 1) for i in range(count - 1)]
        backward = [(target, source) for source, target in forward]
        low = lax.ppermute(
            lax.slice_in_dim(block, block.shape[dim] - width, None, axis=dim), axis, forward
        )
        high = lax.ppermute(lax.slice_in_dim(block, 0, width, axis=dim), axis, backward)
        block = jnp.concatenate([low, block, high], axis=dim)
    return block


def from_behind(block, axis, distance):
    devices = range(lax.axis_size(axis))
    route = [(i - distance, i) for i in devices if i - distance in devices]
    return lax.ppermute(block, axis, route)


def group_sum(value, axis, radices):
    count = lax.axis_size(axis)
    me = lax.axis_index(axis)
    stride = 1
    for radix in radices:
        member = (me // stride) % radix
        received = [value]
        for shift in range(1, radix):
            pairs = []
            for i in range(count):
                base = i - ((i // stride) % radix) * stride
                target = base + (((i // stride) % radix + shift) % radix) * stride
                pairs.append((i, target))
            received.append(lax.ppermute(value, axis, pairs))
        stacked = jnp.stack(received)
        ordered = jnp.take(stacked, (member - jnp.arange(radix)) % radix, axis=0)
        value = ordered[0]
        for j in range(1, radix):
            value = value + ordered[j]
        stride *= radix
    return value


def live_pattern(block_mask, left_live, right_live, block_rows):
    inside = lax.broadcasted_iota(jnp.int32, (block_rows,), 0)
    row_ok = (inside[None, :] < left_live[:, None]).reshape(-1)
    col_ok = (inside[None, :] < right_live[:, None]).reshape(-1)
    expanded = jnp.repeat(jnp.repeat(block_mask, block_rows, axis=0), block_rows, axis=1)
    return (expanded > 0) & row_ok[:, None] & col_ok[None, :]


def on_device(
    psi, env_left, env_right, first_site_operator, mpo_right, block_mask, left_live, right_live
):
    block_rows = env_left.shape[2]
    mpo_width = env_left.shape[4]
    states = psi.shape[1]
    site_states = first_site_operator.shape[2]
    couplings = env_left[0].reshape(3, block_rows, block_rows * mpo_width)
    from_next_row = from_behind(couplings[0], "row", -1)
    from_prev_row = from_behind(couplings[2], "row", 1)
    live_mask = live_pattern(block_mask, left_live, right_live, block_rows)
    masked_wavefunction = psi * live_mask[:, None, :].astype(jnp.bfloat16)
    flat_wavefunction = masked_wavefunction.reshape(block_rows, states * block_rows)
    next_wavefunction = from_behind(flat_wavefunction, "row", -1).astype(jnp.float32)
    prev_wavefunction = from_behind(flat_wavefunction, "row", 1).astype(jnp.float32)
    widened = padded(masked_wavefunction, (("col", 2),), block_rows)
    right_tensor = env_right[0].reshape(3 * block_rows, mpo_width, block_rows)
    section_one = jnp.einsum(
        "xsu,uny->xsny", widened, right_tensor, preferred_element_type=jnp.float32
    ).astype(jnp.bfloat16)
    section_one = section_one.reshape(block_rows, site_states, site_states, mpo_width, block_rows)
    second_section = jnp.einsum(
        "mnts,xasnb->xamtb", mpo_right, section_one, preferred_element_type=jnp.float32
    ).astype(jnp.bfloat16)
    third_section = jnp.einsum(
        "dquo,woqzj->wduzj", first_site_operator, second_section, preferred_element_type=jnp.float32
    ).astype(jnp.bfloat16)
    stacked = jnp.stack([from_next_row, couplings[1], from_prev_row]).reshape(
        3, block_rows, block_rows, mpo_width
    )
    coupled = jnp.einsum(
        "kxvl,vlrty->kxrty", stacked, third_section, preferred_element_type=jnp.float32
    ).reshape(3, block_rows, states * block_rows)
    to_next, own, to_prev = coupled[0], coupled[1], coupled[2]
    from_prev = from_behind(to_next, "row", 1)
    from_next = from_behind(to_prev, "row", -1)
    psi_float = flat_wavefunction.astype(jnp.float32)
    numerator = (
        jnp.sum(psi_float * own)
        + jnp.sum(next_wavefunction * to_next)
        + jnp.sum(prev_wavefunction * to_prev)
    )
    sums = jnp.stack([numerator, jnp.sum(psi_float * psi_float)])
    sums = group_sum(group_sum(sums, "col", (2, 4)), "row", (4, 4))
    quotient = sums[0] / (sums[1] + 1e-06)
    total = own + from_prev + from_next
    live_float = jnp.broadcast_to(
        live_mask[:, None, :], (block_rows, states, block_rows)
    ).reshape(block_rows, states * block_rows).astype(jnp.float32)
    applied = total * live_float
    residual = applied - quotient * psi_float
    shape = (block_rows, states, block_rows)
    return (
        applied.astype(jnp.bfloat16).reshape(shape),
        residual.astype(jnp.bfloat16).reshape(shape),
        quotient,
    )


def solution(mesh):
    return jax.shard_map(
        on_device,
        mesh=mesh,
        in_specs=(
            P("row", None, "col"),
            P("row", None, None, None, None),
            P("col", None, None, None, None),
            P(),
            P(),
            P("row", "col"),
            P("row"),
            P("col"),
        ),
        out_specs=(P("row", None, "col"), P("row", None, "col"), P()),
        check_vma=False,
    )
```

```python
import jax
import jax.numpy as jnp
from jax import lax
from jax.experimental.layout import Layout, with_layout_constraint
from jax.sharding import PartitionSpec as P


def padded(block, sides, width):
    for axis, dim in sides:
        count = lax.axis_size(axis)
        forward = [(i, i + 1) for i in range(count - 1)]
        backward = [(target, source) for source, target in forward]
        low = lax.ppermute(
            lax.slice_in_dim(block, block.shape[dim] - width, None, axis=dim), axis, forward
        )
        high = lax.ppermute(lax.slice_in_dim(block, 0, width, axis=dim), axis, backward)
        block = jnp.concatenate([low, block, high], axis=dim)
    return block


def from_behind(block, axis, distance):
    devices = range(lax.axis_size(axis))
    route = [(i - distance, i) for i in devices if i - distance in devices]
    return lax.ppermute(block, axis, route)


def group_sum(value, axis, radices):
    count = lax.axis_size(axis)
    me = lax.axis_index(axis)
    stride = 1
    for radix in radices:
        member = (me // stride) % radix
        received = [value]
        for shift in range(1, radix):
            pairs = []
            for i in range(count):
                base = i - ((i // stride) % radix) * stride
                target = base + (((i // stride) % radix + shift) % radix) * stride
                pairs.append((i, target))
            received.append(lax.ppermute(value, axis, pairs))
        stacked = jnp.stack(received)
        ordered = jnp.take(stacked, (member - jnp.arange(radix)) % radix, axis=0)
        value = ordered[0]
        for j in range(1, radix):
            value = value + ordered[j]
        stride *= radix
    return value


def live_pattern(block_mask, left_live, right_live, block_rows):
    inside = lax.broadcasted_iota(jnp.int32, (block_rows,), 0)
    row_ok = (inside[None, :] < left_live[:, None]).reshape(-1)
    col_ok = (inside[None, :] < right_live[:, None]).reshape(-1)
    expanded = jnp.repeat(jnp.repeat(block_mask, block_rows, axis=0), block_rows, axis=1)
    return (expanded > 0) & row_ok[:, None] & col_ok[None, :]


def on_device(
    psi, env_left, env_right, first_site_operator, mpo_right, block_mask, left_live, right_live
):
    block_rows = env_left.shape[2]
    mpo_width = env_left.shape[4]
    states = psi.shape[1]
    site_states = first_site_operator.shape[2]
    couplings = env_left[0].reshape(3, block_rows, block_rows * mpo_width)
    from_next_row = from_behind(couplings[0], "row", -1)
    from_prev_row = from_behind(couplings[2], "row", 1)
    live_mask = live_pattern(block_mask, left_live, right_live, block_rows)
    masked_wavefunction = psi * live_mask[:, None, :].astype(jnp.bfloat16)
    flat_wavefunction = masked_wavefunction.reshape(block_rows, states * block_rows)
    next_wavefunction = from_behind(flat_wavefunction, "row", -1).astype(jnp.float32)
    prev_wavefunction = from_behind(flat_wavefunction, "row", 1).astype(jnp.float32)
    widened = padded(masked_wavefunction, (("col", 2),), block_rows)
    right_tensor = env_right[0].reshape(3 * block_rows, mpo_width, block_rows)
    section_one = jnp.einsum(
        "xsu,uny->xsny", widened, right_tensor, preferred_element_type=jnp.float32
    ).astype(jnp.bfloat16)
    section_one = section_one.reshape(block_rows, site_states, site_states, mpo_width, block_rows)
    second_section = jnp.einsum(
        "mnts,xasnb->xamtb", mpo_right, section_one, preferred_element_type=jnp.float32
    ).astype(jnp.bfloat16)
    third_section = jnp.einsum(
        "dquo,woqzj->wduzj", first_site_operator, second_section, preferred_element_type=jnp.float32
    ).astype(jnp.bfloat16)
    stacked = jnp.stack([from_next_row, couplings[1], from_prev_row]).reshape(
        3, block_rows, block_rows, mpo_width
    )
    coupled = jnp.einsum(
        "kxvl,vlrty->kxrty", stacked, third_section, preferred_element_type=jnp.float32
    )
    coupled = with_layout_constraint(coupled, Layout(major_to_minor=(2, 3, 0, 4, 1)))
    coupled = coupled.reshape(3, block_rows, states * block_rows)
    to_next, own, to_prev = coupled[0], coupled[1], coupled[2]
    from_prev = from_behind(to_next, "row", 1)
    from_next = from_behind(to_prev, "row", -1)
    psi_float = flat_wavefunction.astype(jnp.float32)
    numerator = (
        jnp.sum(psi_float * own)
        + jnp.sum(next_wavefunction * to_next)
        + jnp.sum(prev_wavefunction * to_prev)
    )
    sums = jnp.stack([numerator, jnp.sum(psi_float * psi_float)])
    sums = group_sum(group_sum(sums, "col", (2, 4)), "row", (4, 4))
    quotient = sums[0] / (sums[1] + 1e-06)
    total = own + from_prev + from_next
    live_float = jnp.broadcast_to(
        live_mask[:, None, :], (block_rows, states, block_rows)
    ).reshape(block_rows, states * block_rows).astype(jnp.float32)
    applied = total * live_float
    residual = applied - quotient * psi_float
    shape = (block_rows, states, block_rows)
    return (
        applied.astype(jnp.bfloat16).reshape(shape),
        residual.astype(jnp.bfloat16).reshape(shape),
        quotient,
    )


def solution(mesh):
    return jax.shard_map(
        on_device,
        mesh=mesh,
        in_specs=(
            P("row", None, "col"),
            P("row", None, None, None, None),
            P("col", None, None, None, None),
            P(),
            P(),
            P("row", "col"),
            P("row"),
            P("col"),
        ),
        out_specs=(P("row", None, "col"), P("row", None, "col"), P()),
        check_vma=False,
    )
```

```python
import jax
import jax.numpy as jnp
from jax import lax
from jax.experimental.layout import Layout, with_layout_constraint
from jax.sharding import PartitionSpec as P


def padded(block, sides, width):
    for axis, dim in sides:
        count = lax.axis_size(axis)
        forward = [(i, i + 1) for i in range(count - 1)]
        backward = [(target, source) for source, target in forward]
        low = lax.ppermute(
            lax.slice_in_dim(block, block.shape[dim] - width, None, axis=dim), axis, forward
        )
        high = lax.ppermute(lax.slice_in_dim(block, 0, width, axis=dim), axis, backward)
        block = jnp.concatenate([low, block, high], axis=dim)
    return block


def from_behind(block, axis, distance):
    devices = range(lax.axis_size(axis))
    route = [(i - distance, i) for i in devices if i - distance in devices]
    return lax.ppermute(block, axis, route)


def group_sum(value, axis, radices):
    count = lax.axis_size(axis)
    stride = 1
    for radix in radices:
        level = [value]
        for shift in range(1, radix):
            pairs = [(i, i ^ (shift * stride)) for i in range(count)]
            level.append(lax.ppermute(value, axis, pairs))
        while len(level) > 1:
            level = [level[j] + level[j + 1] for j in range(0, len(level), 2)]
        value = level[0]
        stride *= radix
    return value


def live_pattern(block_mask, left_live, right_live, block_rows):
    inside = lax.broadcasted_iota(jnp.int32, (block_rows,), 0)
    row_ok = (inside[None, :] < left_live[:, None]).reshape(-1)
    col_ok = (inside[None, :] < right_live[:, None]).reshape(-1)
    expanded = jnp.repeat(jnp.repeat(block_mask, block_rows, axis=0), block_rows, axis=1)
    return (expanded > 0) & row_ok[:, None] & col_ok[None, :]


def on_device(
    psi, env_left, env_right, first_site_operator, mpo_right, block_mask, left_live, right_live
):
    block_rows = env_left.shape[2]
    mpo_width = env_left.shape[4]
    states = psi.shape[1]
    site_states = first_site_operator.shape[2]
    couplings = env_left[0].reshape(3, block_rows, block_rows * mpo_width)
    from_next_row = from_behind(couplings[0], "row", -1)
    from_prev_row = from_behind(couplings[2], "row", 1)
    live_mask = live_pattern(block_mask, left_live, right_live, block_rows)
    masked_wavefunction = psi * live_mask[:, None, :].astype(jnp.bfloat16)
    flat_wavefunction = masked_wavefunction.reshape(block_rows, states * block_rows)
    next_wavefunction = from_behind(flat_wavefunction, "row", -1).astype(jnp.float32)
    prev_wavefunction = from_behind(flat_wavefunction, "row", 1).astype(jnp.float32)
    widened = padded(masked_wavefunction, (("col", 2),), block_rows)
    right_tensor = env_right[0].reshape(3 * block_rows, mpo_width, block_rows)
    section_one = jnp.einsum(
        "xsu,uny->xsny", widened, right_tensor, preferred_element_type=jnp.float32
    ).astype(jnp.bfloat16)
    section_one = section_one.reshape(block_rows, site_states, site_states, mpo_width, block_rows)
    second_section = jnp.einsum(
        "mnts,xasnb->xamtb", mpo_right, section_one, preferred_element_type=jnp.float32
    ).astype(jnp.bfloat16)
    third_section = jnp.einsum(
        "dquo,woqzj->wduzj", first_site_operator, second_section, preferred_element_type=jnp.float32
    ).astype(jnp.bfloat16)
    stacked = jnp.stack([from_next_row, couplings[1], from_prev_row]).reshape(
        3, block_rows, block_rows, mpo_width
    )
    coupled = jnp.einsum(
        "kxvl,vlrty->kxrty", stacked, third_section, preferred_element_type=jnp.float32
    )
    coupled = with_layout_constraint(coupled, Layout(major_to_minor=(2, 3, 0, 4, 1)))
    coupled = coupled.reshape(3, block_rows, states * block_rows)
    to_next, own, to_prev = coupled[0], coupled[1], coupled[2]
    from_prev = from_behind(to_next, "row", 1)
    from_next = from_behind(to_prev, "row", -1)
    psi_float = flat_wavefunction.astype(jnp.float32)
    numerator = (
        jnp.sum(psi_float * own)
        + jnp.sum(next_wavefunction * to_next)
        + jnp.sum(prev_wavefunction * to_prev)
    )
    sums = jnp.stack([numerator, jnp.sum(psi_float * psi_float)])
    sums = group_sum(group_sum(sums, "col", (8,)), "row", (4, 4))
    quotient = sums[0] / (sums[1] + 1e-06)
    total = own + from_prev + from_next
    live_float = jnp.broadcast_to(
        live_mask[:, None, :], (block_rows, states, block_rows)
    ).reshape(block_rows, states * block_rows).astype(jnp.float32)
    applied = total * live_float
    residual = applied - quotient * psi_float
    shape = (block_rows, states, block_rows)
    return (
        applied.astype(jnp.bfloat16).reshape(shape),
        residual.astype(jnp.bfloat16).reshape(shape),
        quotient,
    )


def solution(mesh):
    return jax.shard_map(
        on_device,
        mesh=mesh,
        in_specs=(
            P("row", None, "col"),
            P("row", None, None, None, None),
            P("col", None, None, None, None),
            P(),
            P(),
            P("row", "col"),
            P("row"),
            P("col"),
        ),
        out_specs=(P("row", None, "col"), P("row", None, "col"), P()),
        check_vma=False,
    )
```

```python
import jax
import jax.numpy as jnp
from jax import lax
from jax.experimental.layout import Layout, with_layout_constraint
from jax.sharding import PartitionSpec as P


def padded(block, sides, width):
    for axis, dim in sides:
        count = lax.axis_size(axis)
        forward = [(i, i + 1) for i in range(count - 1)]
        backward = [(target, source) for source, target in forward]
        low = lax.ppermute(
            lax.slice_in_dim(block, block.shape[dim] - width, None, axis=dim), axis, forward
        )
        high = lax.ppermute(lax.slice_in_dim(block, 0, width, axis=dim), axis, backward)
        block = jnp.concatenate([low, block, high], axis=dim)
    return block


def from_behind(block, axis, distance):
    devices = range(lax.axis_size(axis))
    route = [(i - distance, i) for i in devices if i - distance in devices]
    return lax.ppermute(block, axis, route)


def group_sum(value, axis, radices):
    count = lax.axis_size(axis)
    stride = 1
    for radix in radices:
        level = [value]
        for shift in range(1, radix):
            pairs = [(i, i ^ (shift * stride)) for i in range(count)]
            level.append(lax.ppermute(value, axis, pairs))
        while len(level) > 1:
            level = [level[j] + level[j + 1] for j in range(0, len(level), 2)]
        value = level[0]
        stride *= radix
    return value


def live_pattern(block_mask, left_live, right_live, block_rows):
    inside = lax.broadcasted_iota(jnp.int32, (block_rows,), 0)
    row_ok = (inside[None, :] < left_live[:, None]).reshape(-1)
    col_ok = (inside[None, :] < right_live[:, None]).reshape(-1)
    expanded = jnp.repeat(jnp.repeat(block_mask, block_rows, axis=0), block_rows, axis=1)
    return (expanded > 0) & row_ok[:, None] & col_ok[None, :]


def on_device(
    psi, env_left, env_right, first_site_operator, mpo_right, block_mask, left_live, right_live
):
    block_rows = env_left.shape[2]
    mpo_width = env_left.shape[4]
    states = psi.shape[1]
    site_states = first_site_operator.shape[2]
    couplings = jnp.transpose(env_left[0], (0, 3, 1, 2))
    from_next_row = from_behind(couplings[0], "row", -1)
    from_prev_row = from_behind(couplings[2], "row", 1)
    live_mask = live_pattern(block_mask, left_live, right_live, block_rows)
    masked_wavefunction = psi * live_mask[:, None, :].astype(jnp.bfloat16)
    flat_wavefunction = masked_wavefunction.reshape(block_rows, states * block_rows)
    next_wavefunction = from_behind(flat_wavefunction, "row", -1).astype(jnp.float32)
    prev_wavefunction = from_behind(flat_wavefunction, "row", 1).astype(jnp.float32)
    widened = padded(masked_wavefunction, (("col", 2),), block_rows)
    right_tensor = env_right[0].reshape(3 * block_rows, mpo_width, block_rows)
    section_one = jnp.einsum(
        "xsu,uny->xsny", widened, right_tensor, preferred_element_type=jnp.float32
    ).astype(jnp.bfloat16)
    section_one = section_one.reshape(block_rows, site_states, site_states, mpo_width, block_rows)
    second_section = jnp.einsum(
        "mnts,xasnb->xamtb", mpo_right, section_one, preferred_element_type=jnp.float32
    ).astype(jnp.bfloat16)
    third_section = jnp.einsum(
        "dquo,woqzj->wduzj", first_site_operator, second_section, preferred_element_type=jnp.float32
    ).astype(jnp.bfloat16)
    stacked = jnp.stack([from_next_row, couplings[1], from_prev_row])
    coupled = jnp.einsum(
        "klxv,vlrty->kxrty", stacked, third_section, preferred_element_type=jnp.float32
    )
    coupled = with_layout_constraint(coupled, Layout(major_to_minor=(2, 3, 0, 4, 1)))
    coupled = coupled.reshape(3, block_rows, states * block_rows)
    to_next, own, to_prev = coupled[0], coupled[1], coupled[2]
    from_prev = from_behind(to_next, "row", 1)
    from_next = from_behind(to_prev, "row", -1)
    psi_float = flat_wavefunction.astype(jnp.float32)
    numerator = (
        jnp.sum(psi_float * own)
        + jnp.sum(next_wavefunction * to_next)
        + jnp.sum(prev_wavefunction * to_prev)
    )
    sums = jnp.stack([numerator, jnp.sum(psi_float * psi_float)])
    sums = group_sum(group_sum(sums, "col", (8,)), "row", (4, 4))
    quotient = sums[0] / (sums[1] + 1e-06)
    total = own + from_prev + from_next
    live_float = jnp.broadcast_to(
        live_mask[:, None, :], (block_rows, states, block_rows)
    ).reshape(block_rows, states * block_rows).astype(jnp.float32)
    applied = total * live_float
    residual = applied - quotient * psi_float
    shape = (block_rows, states, block_rows)
    return (
        applied.astype(jnp.bfloat16).reshape(shape),
        residual.astype(jnp.bfloat16).reshape(shape),
        quotient,
    )


def solution(mesh):
    return jax.shard_map(
        on_device,
        mesh=mesh,
        in_specs=(
            P("row", None, "col"),
            P("row", None, None, None, None),
            P("col", None, None, None, None),
            P(),
            P(),
            P("row", "col"),
            P("row"),
            P("col"),
        ),
        out_specs=(P("row", None, "col"), P("row", None, "col"), P()),
        check_vma=False,
    )
```
